256 devices in a mesh: dp: 2 (over z_lo), expert: 32 (over y, z_hi, core), tensor: 4 (over x).
Axes of the slice: x: 4, y: 4, z: 8 (z_hi: 4, z_lo: 2; z = z_hi * 2 + z_lo), core: 2. Of those that a mesh axis runs over, the one named last changes fastest.
Arguments:
- context: bfloat16 [8192, 2048], P(('dp', 'expert'), 'tensor'), may hold values from -6 to 6
- residual: bfloat16 [8192, 2048], P(('dp', 'expert')), may hold values from -6 to 6
- wo_rows: bfloat16 [2048, 2048], P('tensor'), may hold values from -0.125 to 0.125
- norm_gain: float32 [2048], replicated, may hold values from 0.25 to 1.75
- analyzer_out: bfloat16 [8192, 2048], P(('dp', 'expert'), 'tensor'), may hold values from -6 to 6
- gate_probs: float32 [8192, 6], P(('dp', 'expert')), may hold values from 0.05 to 0.5
- expert_ids: int32 [8192, 6], P(('dp', 'expert')), may hold values from 0 to 63, all different within a row; in each aligned block of 128 rows (0 to 127, 128 to 255, ...) at most 14 rows name the same one
- w_gate_up: bfloat16 [64, 2, 2048, 1408], P('expert', None, 'dp', 'tensor'), may hold values from -0.125 to 0.125
- w_down: bfloat16 [64, 1408, 2048], P('expert', 'tensor', 'dp'), may hold values from -0.15625 to 0.15625
Outputs:
- block_out: bfloat16 [8192, 2048], P(('dp', 'expert'), 'tensor')
- context_grad: bfloat16 [8192, 2048], P(('dp', 'expert'), 'tensor')
- gate_prob_grad: float32 [8192, 6], P(('dp', 'expert'))
- gate_up_grad: bfloat16 [64, 2, 2048, 1408], P('expert', None, 'dp', 'tensor')
- down_grad: bfloat16 [64, 1408, 2048], P('expert', 'tensor', 'dp')
The draws below stay inside these ranges and needn't reach their ends.
Inputs may be any that keep to these rules, and one draw needn't show every extreme that they name: `expert_ids`: each row names 6 different experts; within each device's rows (aligned blocks of 128 rows) no expert is named more than 14 times, a bound that some block reaches.
All inputs are finite; a program needn't handle non-finite values.
Results may differ from the reference program's by a relative error of at most 0.024.
Values may be sent and summed in bfloat16 or wider, within the bound.
No kernel may reach another device: no remote copies, remote signals or barrier semaphores. Data moves between devices by JAX's collectives and lax.ppermute only.
A program may use at most 128 MiB of HBM per device.

```python
import math
import jax
import jax.numpy as jnp
import numpy as np
from jax import lax

D = 2048
FF = 1408
EXPERTS = 64
TOP = 6
TOK_DEV = 128
CAP = 14
TOKENS = 8192
N_DP = 2
N_EXPERT = 32
N_TENSOR = 4


def block_scale(stream_key, dims, shards, least, top_value):
    def one(position, shards_of):
        heights = jax.random.uniform(jax.random.fold_in(jax.random.fold_in(stream_key, 6), position), (shards_of,), jnp.float32, least / len(shards), top_value / len(shards))
        return jnp.repeat(jnp.exp(heights), dims[position] // shards_of).reshape((-1,) + (1,) * (len(dims) - position - 1))

    gain = one(*shards[0])
    for cut in shards[1:]:
        gain = gain * one(*cut)
    return gain


def shared_out(rng, own, number, rows, count, top, most, lean):
    order = jax.random.permutation(rng, count)
    crowded, ordinary = load_shares(count, rows * top, most, lean, True), load_shares(count, rows * top, most, lean, False)
    places = jnp.arange(count)

    def named(tallies, rotation):
        used = int((tallies > 0).sum())
        fixed = max(1, used // 4)
        shifted = fixed + (places - fixed + rotation * (used - fixed)) % max(1, count - fixed)
        return jnp.zeros((count,), jnp.int32).at[order[jnp.where(places < fixed, places, shifted)]].set(jnp.asarray(tallies, jnp.int32))

    tallies = jnp.where(number % 4 == 0, named(crowded, number // 4), named(ordinary, number - number // 4 - 1))
    mixed = jax.random.permutation(jax.random.fold_in(own, 3), count)
    source_of, receiver = mixed[0:count // 2 * 2:2], mixed[1:count // 2 * 2:2]
    slack = jnp.minimum(tallies[source_of] - 1, most - tallies[receiver]) // 2
    slack = jnp.where((source_of == order[0]) | (receiver == order[0]) | (tallies[receiver] == 0), 0, jnp.maximum(slack, 0))
    shifted = jax.random.randint(jax.random.fold_in(own, 4), (count // 2,), 0, 1 << 20) % (slack + 1)
    tallies = tallies.at[source_of].add(-shifted).at[receiver].add(shifted)
    labels = jnp.searchsorted(jnp.cumsum(tallies), jnp.arange(rows * top), side="right").astype(jnp.int32)
    table = labels.reshape(top, rows).T
    table = table[jax.random.permutation(jax.random.fold_in(own, 1), rows)]
    rotation = jax.random.randint(jax.random.fold_in(own, 2), (rows, 1), 0, top)
    return jnp.take_along_axis(table, (jnp.arange(top)[None, :] + rotation) % top, axis=1)


def load_shares(amount, total, limit, slope, full):
    loads = [(1 << 20) // math.isqrt(standing ** slope) + 1 for standing in range(1, amount + 1)]
    largest = limit if full else min(limit, max(-(-total // amount), total * loads[0] // sum(loads)))
    least = 1 if total - largest >= amount - 1 else 0
    holding, surplus = [largest] + [least] * (amount - 1), total - largest - least * (amount - 1)
    while surplus > 0:
        movable = [i for i in range(1, amount) if holding[i] < largest] or [i for i in range(1, amount) if holding[i] < limit]
        mass, remaining = sum([loads[i] for i in movable]), surplus
        for i in movable:
            extra = min(limit - holding[i], max(1, remaining * loads[i] // mass), surplus)
            holding[i] = holding[i] + extra
            surplus = surplus - extra
    return np.array(holding)


def centred(own_key, extent, scale, limit, pieces=(), kind=jnp.bfloat16):
    values = scale * jax.random.normal(own_key, extent, jnp.float32)
    if pieces:
        values = values * block_scale(own_key, extent, pieces, -0.22, 0.18)
    return jnp.clip(values, -limit, limit).astype(kind)


def setup_inputs(seed: int = 0) -> dict:
    keys = jax.random.split(jax.random.key(seed), 10)
    context = centred(keys[0], (TOKENS, D), 1.0, 6.0, ((0, 64), (1, 4)))
    residual = centred(keys[1], (TOKENS, D), 1.0, 6.0, ((0, 64),))
    wo_rows = centred(keys[2], (D, D), D ** -0.5, 0.125, ((0, 4),))
    norm_gain = jnp.clip(1.0 + 0.15 * jax.random.normal(keys[3], (D,), jnp.float32), 0.25, 1.75)
    analyzer_out = centred(keys[4], (TOKENS, D), 1.0, 6.0, ((0, 64), (1, 4)))
    gate_probs = jnp.clip(jnp.exp(math.log(0.5) - 2.3025851 * jax.random.uniform(keys[5], (TOKENS, TOP), jnp.float32) ** block_scale(keys[5], (TOKENS, TOP), ((0, 64),), -0.2, 0.2)), 0.05, 0.5)
    expert_ids_keys = jax.random.split(jax.random.fold_in(keys[6], 1), TOKENS // TOK_DEV)
    expert_ids_turns = jax.random.permutation(jax.random.fold_in(keys[6], 3), TOKENS // TOK_DEV)
    expert_ids = jax.vmap(lambda own, number: shared_out(jax.random.fold_in(keys[6], 2), own, number, TOK_DEV, EXPERTS, TOP, CAP, 1))(expert_ids_keys, expert_ids_turns).reshape((TOKENS, TOP))
    w_gate_up = centred(keys[7], (EXPERTS, 2, D, FF), D ** -0.5, 0.125, ((0, 32), (2, 2), (3, 4)))
    w_down = centred(keys[8], (EXPERTS, FF, D), FF ** -0.5, 0.15625, ((0, 32), (1, 4), (2, 2)))
    return {"context": context, "residual": residual, "wo_rows": wo_rows, "norm_gain": norm_gain, "analyzer_out": analyzer_out, "gate_probs": gate_probs, "expert_ids": expert_ids, "w_gate_up": w_gate_up, "w_down": w_down}


NORM_EPS = 1e-06
LOSS_WEIGHT = 0.25

def rounded_add(summed, term):
    held = lax.optimization_barrier(term.astype(jnp.bfloat16))
    return summed + held.astype(jnp.float32)

def tensor_summed(pairs):
    slice_width = pairs[0][0].shape[1] // N_TENSOR
    summed = jnp.zeros((pairs[0][0].shape[0], pairs[0][1].shape[1]), jnp.float32)
    for member in range(N_TENSOR):
        lower = member * slice_width
        term = jnp.zeros_like(summed)
        for left, right in pairs:
            term = term + jnp.dot(left[:, lower:lower + slice_width], right[lower:lower + slice_width], preferred_element_type=jnp.float32)
        summed = rounded_add(summed, term)
    return summed.astype(jnp.bfloat16)

def data_summed(left, right):
    half_rows = N_EXPERT * CAP
    summed = jnp.zeros((left.shape[1], right.shape[1]), jnp.float32)
    for member in range(N_DP):
        lower = member * half_rows
        term = jnp.dot(left[lower:lower + half_rows].T, right[lower:lower + half_rows], preferred_element_type=jnp.float32)
        summed = rounded_add(summed, term)
    return summed.astype(jnp.bfloat16)

def reference(context, residual, wo_rows, norm_gain, analyzer_out, gate_probs, expert_ids, w_gate_up, w_down):
    tok_count, top_count = expert_ids.shape
    feature_count = residual.shape[1]
    group_count = tok_count // TOK_DEV
    row_count = group_count * CAP
    entry_count = tok_count * top_count
    hidden_in = residual.astype(jnp.float32) + jnp.dot(context, wo_rows, preferred_element_type=jnp.float32)
    inv_rms = lax.rsqrt(lax.optimization_barrier(jnp.mean(hidden_in * hidden_in, axis=1, keepdims=True)) + NORM_EPS)
    normed = (norm_gain * hidden_in * inv_rms).astype(jnp.bfloat16)
    grouped = expert_ids.reshape(group_count, TOK_DEV * top_count)
    onehot = (grouped[:, :, None] == jnp.arange(EXPERTS, dtype=jnp.int32)[None, None, :]).astype(jnp.int32)
    slot_index = lax.optimization_barrier(jnp.sum((jnp.cumsum(onehot, axis=1) - onehot) * onehot, axis=2)).reshape(-1)
    flat_ids = expert_ids.reshape(-1)
    entry_group = jnp.arange(entry_count, dtype=jnp.int32) // (TOK_DEV * top_count)
    normed_pad = jnp.concatenate([normed, jnp.zeros((1, feature_count), jnp.bfloat16)], axis=0)
    gate_pad = jnp.concatenate([gate_probs.reshape(-1), jnp.zeros((1,), jnp.float32)])

    def rows_of(expert):
        place = jnp.where(flat_ids == expert, entry_group * CAP + slot_index, row_count).astype(jnp.int32)
        empty = jnp.full((row_count,), entry_count, jnp.int32)
        return empty.at[place].set(jnp.arange(entry_count, dtype=jnp.int32), mode='drop')

    def expert_apply(expert, row_entry):
        row_token = row_entry // top_count
        rows = normed_pad[row_token]
        pre_gate = jnp.dot(rows, w_gate_up[expert, 0], preferred_element_type=jnp.float32)
        pre_up = jnp.dot(rows, w_gate_up[expert, 1], preferred_element_type=jnp.float32)
        activation = (jax.nn.silu(pre_gate) * pre_up).astype(jnp.bfloat16)
        expert_out = tensor_summed([(activation, w_down[expert])])
        return (row_token, rows, pre_gate, pre_up, activation, expert_out)

    def forward_step(mixed, expert):
        row_entry = rows_of(expert)
        row_token, rows, pre_gate, pre_up, activation, expert_out = expert_apply(expert, row_entry)
        weighted = gate_pad[row_entry][:, None] * expert_out.astype(jnp.float32)
        return (mixed.at[row_token].add(weighted, mode='drop'), None)
    mixed, ignored = lax.scan(forward_step, jnp.zeros((tok_count, feature_count), jnp.float32), jnp.arange(EXPERTS, dtype=jnp.int32))
    block_out = (hidden_in + mixed).astype(jnp.bfloat16)
    error = (LOSS_WEIGHT * (block_out.astype(jnp.float32) - analyzer_out.astype(jnp.float32))).astype(jnp.bfloat16)
    error_pad = jnp.concatenate([error, jnp.zeros((1, feature_count), jnp.bfloat16)], axis=0)

    def backward_step(carry, expert):
        d_normed, gate_flat = carry
        row_entry = rows_of(expert)
        row_token, rows, pre_gate, pre_up, activation, expert_out = expert_apply(expert, row_entry)
        row_error = error_pad[row_token].astype(jnp.float32)
        gate_flat = gate_flat.at[row_entry].set(lax.optimization_barrier(jnp.sum(row_error * expert_out.astype(jnp.float32), axis=1)))
        grad_slot = (gate_pad[row_entry][:, None] * row_error).astype(jnp.bfloat16)
        down_part = data_summed(activation, grad_slot)
        d_act = jnp.dot(grad_slot, w_down[expert].T, preferred_element_type=jnp.float32)
        sigmoid_pre = jax.nn.sigmoid(pre_gate)
        d_gate_pre = (d_act * pre_up * sigmoid_pre * (1.0 + pre_gate * (1.0 - sigmoid_pre))).astype(jnp.bfloat16)
        d_up_pre = (d_act * pre_gate * sigmoid_pre).astype(jnp.bfloat16)
        gate_part = data_summed(rows, d_gate_pre)
        up_part = data_summed(rows, d_up_pre)
        d_rows = tensor_summed([(d_gate_pre, w_gate_up[expert, 0].T), (d_up_pre, w_gate_up[expert, 1].T)])
        d_normed = d_normed.at[row_token].add(d_rows.astype(jnp.float32), mode='drop')
        return ((d_normed, gate_flat), (jnp.stack([gate_part, up_part], axis=0), down_part))
    start_carry = (jnp.zeros((tok_count, feature_count), jnp.float32), jnp.zeros((entry_count + 1,), jnp.float32))
    (d_normed, gate_flat), (gate_up_grad, down_grad) = lax.scan(backward_step, start_carry, jnp.arange(EXPERTS, dtype=jnp.int32))
    scaled = norm_gain * d_normed
    norm_dots = lax.optimization_barrier(jnp.sum(scaled * hidden_in, axis=1, keepdims=True))
    cubed = inv_rms * inv_rms * inv_rms
    d_hidden = (error.astype(jnp.float32) + inv_rms * scaled - hidden_in * cubed * norm_dots / feature_count).astype(jnp.bfloat16)
    context_grad = jnp.dot(d_hidden, wo_rows.T, preferred_element_type=jnp.float32).astype(jnp.bfloat16)
    gate_prob_grad = gate_flat[:entry_count].reshape(tok_count, top_count)
    return (block_out, context_grad, gate_prob_grad, gate_up_grad, down_grad)
```

```python
import jax
import jax.numpy as jnp
from jax import lax
from jax.sharding import PartitionSpec as P

EXPERTS = 64
CAP = 14


NORM_EPS = 1e-06
LOSS_WEIGHT = 0.25


def to_experts(outgoing):
    return lax.all_to_all(outgoing, "expert", split_axis=1, concat_axis=1, tiled=True)


def to_tokens(outgoing):
    return lax.all_to_all(outgoing, "expert", split_axis=1, concat_axis=1, tiled=True)


def weight_terms(arrived, activation, grad_in, d_gate_pre, d_up_pre):
    down_part = jnp.einsum(
        "escf,escd->efd", activation, grad_in, preferred_element_type=jnp.float32
    )
    gate_part = jnp.einsum(
        "escd,escf->edf", arrived, d_gate_pre, preferred_element_type=jnp.float32
    )
    up_part = jnp.einsum("escd,escf->edf", arrived, d_up_pre, preferred_element_type=jnp.float32)
    return (jnp.stack([gate_part, up_part], axis=1), down_part)


def per_device(
    context, residual, wo_rows, norm_gain, analyzer_out, gate_probs, expert_ids, w_gate_up, w_down
):
    tok_count, top_count = expert_ids.shape
    feature_count = residual.shape[1]
    tensor_count = lax.axis_size("tensor")
    expert_ranks = lax.axis_size("expert")
    col_count = feature_count // tensor_count
    col_start = lax.axis_index("tensor") * col_count
    local_experts = w_gate_up.shape[0]
    slot_count = EXPERTS * CAP
    expert_range = jnp.arange(EXPERTS, dtype=jnp.int32)
    slot_order = expert_range % local_experts * expert_ranks + expert_range // local_experts
    gate_up_full, down_full = (
        lax.all_gather(w_gate_up, "dp", axis=2, tiled=True),
        lax.all_gather(w_down, "dp", axis=2, tiled=True),
    )
    partial_attn = jnp.dot(context, wo_rows, preferred_element_type=jnp.float32)
    attn_cols = lax.psum_scatter(
        partial_attn.astype(jnp.bfloat16), "tensor", scatter_dimension=1, tiled=True
    )
    hidden_cols = lax.dynamic_slice_in_dim(residual, col_start, col_count, 1).astype(
        jnp.float32
    ) + attn_cols.astype(jnp.float32)
    square_sum = lax.psum(jnp.sum(hidden_cols * hidden_cols, axis=1, keepdims=True), "tensor")
    inv_rms = lax.rsqrt(square_sum / feature_count + NORM_EPS)
    gain_cols = lax.dynamic_slice_in_dim(norm_gain, col_start, col_count, 0)
    normed = (gain_cols * hidden_cols * inv_rms).astype(jnp.bfloat16)
    flat_ids = expert_ids.reshape(-1)
    onehot = (flat_ids[:, None] == expert_range[None, :]).astype(jnp.int32)
    slot_index = jnp.sum((jnp.cumsum(onehot, axis=0) - onehot) * onehot, axis=1)
    expert_slot = jnp.sum(onehot * slot_order[None, :], axis=1)
    dest_row = expert_slot * CAP + slot_index
    sentinel = tok_count * top_count
    row_entry = (
        jnp.full((slot_count,), sentinel, jnp.int32)
        .at[dest_row]
        .set(jnp.arange(sentinel, dtype=jnp.int32))
    )
    row_token = row_entry // top_count
    gate_pad = jnp.concatenate([gate_probs.reshape(-1), jnp.zeros((1,), jnp.float32)])
    row_gate = gate_pad[row_entry]
    normed_pad = jnp.concatenate([normed, jnp.zeros((1, col_count), jnp.bfloat16)], axis=0)
    outgoing = normed_pad[row_token].reshape(local_experts, expert_ranks, CAP, col_count)
    arrived = lax.all_gather(to_experts(outgoing), "tensor", axis=3, tiled=True)
    gate_full = gate_up_full[:, 0]
    up_full = gate_up_full[:, 1]
    pre_gate = jnp.einsum("escd,edf->escf", arrived, gate_full, preferred_element_type=jnp.float32)
    pre_up = jnp.einsum("escd,edf->escf", arrived, up_full, preferred_element_type=jnp.float32)
    activation = (jax.nn.silu(pre_gate) * pre_up).astype(jnp.bfloat16)
    partial_out = jnp.einsum(
        "escf,efd->escd", activation, down_full, preferred_element_type=jnp.float32
    )
    summed_out = lax.psum_scatter(
        partial_out.astype(jnp.bfloat16), "tensor", scatter_dimension=3, tiled=True
    )
    returned = to_tokens(summed_out).reshape(slot_count, col_count)
    entry_out = returned[dest_row].reshape(tok_count, top_count, col_count).astype(jnp.float32)
    block_out = (hidden_cols + jnp.sum(gate_probs[:, :, None] * entry_out, axis=1)).astype(
        jnp.bfloat16
    )
    error = (
        LOSS_WEIGHT * (block_out.astype(jnp.float32) - analyzer_out.astype(jnp.float32))
    ).astype(jnp.bfloat16)
    gate_partial = jnp.sum(error.astype(jnp.float32)[:, None, :] * entry_out, axis=2)
    error_pad = jnp.concatenate([error, jnp.zeros((1, col_count), jnp.bfloat16)], axis=0)
    grad_slot = (row_gate[:, None] * error_pad[row_token].astype(jnp.float32)).astype(jnp.bfloat16)
    grad_slot = grad_slot.reshape(local_experts, expert_ranks, CAP, col_count)
    grad_in = lax.all_gather(to_experts(grad_slot), "tensor", axis=3, tiled=True)
    d_act = jnp.einsum("escd,efd->escf", grad_in, down_full, preferred_element_type=jnp.float32)
    sigmoid_pre = jax.nn.sigmoid(pre_gate)
    d_gate_pre = (d_act * pre_up * sigmoid_pre * (1.0 + pre_gate * (1.0 - sigmoid_pre))).astype(
        jnp.bfloat16
    )
    d_up_pre = (d_act * pre_gate * sigmoid_pre).astype(jnp.bfloat16)
    d_entry_part = jnp.einsum(
        "escf,edf->escd", d_gate_pre, gate_full, preferred_element_type=jnp.float32
    )
    d_entry_part = d_entry_part + jnp.einsum(
        "escf,edf->escd", d_up_pre, up_full, preferred_element_type=jnp.float32
    )
    d_entry_sum = lax.psum_scatter(
        d_entry_part.astype(jnp.bfloat16), "tensor", scatter_dimension=3, tiled=True
    )
    d_returned = to_tokens(d_entry_sum).reshape(slot_count, col_count)
    d_normed = jnp.sum(
        d_returned[dest_row].reshape(tok_count, top_count, col_count).astype(jnp.float32), axis=1
    )
    scaled = gain_cols * d_normed
    norm_partial = jnp.sum(scaled * hidden_cols, axis=1)
    norm_dots, gate_prob_grad = lax.psum((norm_partial, gate_partial), "tensor")
    cubed = inv_rms * inv_rms * inv_rms
    d_hidden = (
        error.astype(jnp.float32)
        + inv_rms * scaled
        - hidden_cols * cubed * norm_dots[:, None] / feature_count
    ).astype(jnp.bfloat16)
    context_grad = lax.dot_general(
        lax.all_gather(d_hidden, "tensor", axis=1, tiled=True),
        wo_rows,
        (((1,), (1,)), ((), ())),
        preferred_element_type=jnp.float32,
    ).astype(jnp.bfloat16)
    gate_up_part, down_part = weight_terms(arrived, activation, grad_in, d_gate_pre, d_up_pre)
    gate_up_grad, down_grad = (
        lax.psum_scatter(
            gate_up_part.astype(jnp.bfloat16), "dp", scatter_dimension=2, tiled=True
        ).astype(jnp.float32),
        lax.psum_scatter(
            down_part.astype(jnp.bfloat16), "dp", scatter_dimension=2, tiled=True
        ).astype(jnp.float32),
    )
    return (
        block_out,
        context_grad,
        gate_prob_grad,
        gate_up_grad.astype(jnp.bfloat16),
        down_grad.astype(jnp.bfloat16),
    )


def solution(mesh):
    in_specs = (
        P(("dp", "expert"), "tensor"),
        P(("dp", "expert"), None),
        P("tensor", None),
        P(),
        P(("dp", "expert"), "tensor"),
        P(("dp", "expert"), None),
        P(("dp", "expert"), None),
        P("expert", None, "dp", "tensor"),
        P("expert", "tensor", "dp"),
    )
    out_specs = (
        P(("dp", "expert"), "tensor"),
        P(("dp", "expert"), "tensor"),
        P(("dp", "expert"), None),
        P("expert", None, "dp", "tensor"),
        P("expert", "tensor", "dp"),
    )
    return jax.shard_map(
        per_device, mesh=mesh, in_specs=in_specs, out_specs=out_specs, check_vma=False
    )
```

```python
import jax
import jax.numpy as jnp
from jax import lax
from jax.sharding import PartitionSpec as P

EXPERTS = 64
CAP = 14


NORM_EPS = 1e-06
LOSS_WEIGHT = 0.25


def to_experts(outgoing):
    return lax.all_to_all(outgoing, "expert", split_axis=1, concat_axis=1, tiled=True)


def to_tokens(outgoing):
    return lax.all_to_all(outgoing, "expert", split_axis=1, concat_axis=1, tiled=True)


DP_SWAP = [(0, 1), (1, 0)]


def dp_joined(own, dp_first, axis):
    other = lax.ppermute(own, "dp", DP_SWAP)
    return jnp.where(
        dp_first,
        jnp.concatenate([own, other], axis=axis),
        jnp.concatenate([other, own], axis=axis),
    )


def dp_halves_summed(part, dp_first, axis):
    half = part.shape[axis] // 2
    low = lax.slice_in_dim(part, 0, half, axis=axis).astype(jnp.bfloat16)
    high = lax.slice_in_dim(part, half, 2 * half, axis=axis).astype(jnp.bfloat16)
    kept = jnp.where(dp_first, low, high)
    arrived = lax.ppermute(jnp.where(dp_first, high, low), "dp", DP_SWAP)
    return kept.astype(jnp.float32) + arrived.astype(jnp.float32)


def weight_terms(arrived, activation, grad_in, d_gate_pre, d_up_pre):
    down_part = jnp.einsum(
        "escf,escd->efd", activation, grad_in, preferred_element_type=jnp.float32
    )
    gate_part = jnp.einsum(
        "escd,escf->edf", arrived, d_gate_pre, preferred_element_type=jnp.float32
    )
    up_part = jnp.einsum("escd,escf->edf", arrived, d_up_pre, preferred_element_type=jnp.float32)
    return (jnp.stack([gate_part, up_part], axis=1), down_part)


def per_device(
    context, residual, wo_rows, norm_gain, analyzer_out, gate_probs, expert_ids, w_gate_up, w_down
):
    tok_count, top_count = expert_ids.shape
    feature_count = residual.shape[1]
    tensor_count = lax.axis_size("tensor")
    expert_ranks = lax.axis_size("expert")
    col_count = feature_count // tensor_count
    col_start = lax.axis_index("tensor") * col_count
    local_experts = w_gate_up.shape[0]
    slot_count = EXPERTS * CAP
    expert_range = jnp.arange(EXPERTS, dtype=jnp.int32)
    slot_order = expert_range % local_experts * expert_ranks + expert_range // local_experts
    dp_first = lax.axis_index("dp") == 0
    gate_up_full, down_full = (
        dp_joined(w_gate_up, dp_first, 2),
        dp_joined(w_down, dp_first, 2),
    )
    partial_attn = jnp.dot(context, wo_rows, preferred_element_type=jnp.float32)
    attn_cols = lax.psum_scatter(
        partial_attn.astype(jnp.bfloat16), "tensor", scatter_dimension=1, tiled=True
    )
    hidden_cols = lax.dynamic_slice_in_dim(residual, col_start, col_count, 1).astype(
        jnp.float32
    ) + attn_cols.astype(jnp.float32)
    square_sum = lax.psum(jnp.sum(hidden_cols * hidden_cols, axis=1, keepdims=True), "tensor")
    inv_rms = lax.rsqrt(square_sum / feature_count + NORM_EPS)
    gain_cols = lax.dynamic_slice_in_dim(norm_gain, col_start, col_count, 0)
    normed = (gain_cols * hidden_cols * inv_rms).astype(jnp.bfloat16)
    flat_ids = expert_ids.reshape(-1)
    onehot = (flat_ids[:, None] == expert_range[None, :]).astype(jnp.int32)
    slot_index = jnp.sum((jnp.cumsum(onehot, axis=0) - onehot) * onehot, axis=1)
    expert_slot = jnp.sum(onehot * slot_order[None, :], axis=1)
    dest_row = expert_slot * CAP + slot_index
    sentinel = tok_count * top_count
    row_entry = (
        jnp.full((slot_count,), sentinel, jnp.int32)
        .at[dest_row]
        .set(jnp.arange(sentinel, dtype=jnp.int32))
    )
    row_token = row_entry // top_count
    gate_pad = jnp.concatenate([gate_probs.reshape(-1), jnp.zeros((1,), jnp.float32)])
    row_gate = gate_pad[row_entry]
    normed_pad = jnp.concatenate([normed, jnp.zeros((1, col_count), jnp.bfloat16)], axis=0)
    outgoing = normed_pad[row_token].reshape(local_experts, expert_ranks, CAP, col_count)
    arrived = lax.all_gather(to_experts(outgoing), "tensor", axis=3, tiled=True)
    gate_full = gate_up_full[:, 0]
    up_full = gate_up_full[:, 1]
    pre_gate = jnp.einsum("escd,edf->escf", arrived, gate_full, preferred_element_type=jnp.float32)
    pre_up = jnp.einsum("escd,edf->escf", arrived, up_full, preferred_element_type=jnp.float32)
    activation = (jax.nn.silu(pre_gate) * pre_up).astype(jnp.bfloat16)
    partial_out = jnp.einsum(
        "escf,efd->escd", activation, down_full, preferred_element_type=jnp.float32
    )
    summed_out = lax.psum_scatter(
        partial_out.astype(jnp.bfloat16), "tensor", scatter_dimension=3, tiled=True
    )
    returned = to_tokens(summed_out).reshape(slot_count, col_count)
    entry_out = returned[dest_row].reshape(tok_count, top_count, col_count).astype(jnp.float32)
    block_out = (hidden_cols + jnp.sum(gate_probs[:, :, None] * entry_out, axis=1)).astype(
        jnp.bfloat16
    )
    error = (
        LOSS_WEIGHT * (block_out.astype(jnp.float32) - analyzer_out.astype(jnp.float32))
    ).astype(jnp.bfloat16)
    gate_partial = jnp.sum(error.astype(jnp.float32)[:, None, :] * entry_out, axis=2)
    error_pad = jnp.concatenate([error, jnp.zeros((1, col_count), jnp.bfloat16)], axis=0)
    grad_slot = (row_gate[:, None] * error_pad[row_token].astype(jnp.float32)).astype(jnp.bfloat16)
    grad_slot = grad_slot.reshape(local_experts, expert_ranks, CAP, col_count)
    grad_in = lax.all_gather(to_experts(grad_slot), "tensor", axis=3, tiled=True)
    d_act = jnp.einsum("escd,efd->escf", grad_in, down_full, preferred_element_type=jnp.float32)
    sigmoid_pre = jax.nn.sigmoid(pre_gate)
    d_gate_pre = (d_act * pre_up * sigmoid_pre * (1.0 + pre_gate * (1.0 - sigmoid_pre))).astype(
        jnp.bfloat16
    )
    d_up_pre = (d_act * pre_gate * sigmoid_pre).astype(jnp.bfloat16)
    d_entry_part = jnp.einsum(
        "escf,edf->escd", d_gate_pre, gate_full, preferred_element_type=jnp.float32
    )
    d_entry_part = d_entry_part + jnp.einsum(
        "escf,edf->escd", d_up_pre, up_full, preferred_element_type=jnp.float32
    )
    d_entry_sum = lax.psum_scatter(
        d_entry_part.astype(jnp.bfloat16), "tensor", scatter_dimension=3, tiled=True
    )
    d_returned = to_tokens(d_entry_sum).reshape(slot_count, col_count)
    d_normed = jnp.sum(
        d_returned[dest_row].reshape(tok_count, top_count, col_count).astype(jnp.float32), axis=1
    )
    scaled = gain_cols * d_normed
    norm_partial = jnp.sum(scaled * hidden_cols, axis=1)
    norm_dots, gate_prob_grad = lax.psum((norm_partial, gate_partial), "tensor")
    cubed = inv_rms * inv_rms * inv_rms
    d_hidden = (
        error.astype(jnp.float32)
        + inv_rms * scaled
        - hidden_cols * cubed * norm_dots[:, None] / feature_count
    ).astype(jnp.bfloat16)
    context_grad = lax.dot_general(
        lax.all_gather(d_hidden, "tensor", axis=1, tiled=True),
        wo_rows,
        (((1,), (1,)), ((), ())),
        preferred_element_type=jnp.float32,
    ).astype(jnp.bfloat16)
    gate_up_part, down_part = weight_terms(arrived, activation, grad_in, d_gate_pre, d_up_pre)
    gate_up_grad, down_grad = (
        dp_halves_summed(gate_up_part, dp_first, 2),
        dp_halves_summed(down_part, dp_first, 2),
    )
    return (
        block_out,
        context_grad,
        gate_prob_grad,
        gate_up_grad.astype(jnp.bfloat16),
        down_grad.astype(jnp.bfloat16),
    )


def solution(mesh):
    in_specs = (
        P(("dp", "expert"), "tensor"),
        P(("dp", "expert"), None),
        P("tensor", None),
        P(),
        P(("dp", "expert"), "tensor"),
        P(("dp", "expert"), None),
        P(("dp", "expert"), None),
        P("expert", None, "dp", "tensor"),
        P("expert", "tensor", "dp"),
    )
    out_specs = (
        P(("dp", "expert"), "tensor"),
        P(("dp", "expert"), "tensor"),
        P(("dp", "expert"), None),
        P("expert", None, "dp", "tensor"),
        P("expert", "tensor", "dp"),
    )
    return jax.shard_map(
        per_device, mesh=mesh, in_specs=in_specs, out_specs=out_specs, check_vma=False
    )
```

```python
import jax
import jax.numpy as jnp
from jax import lax
from jax.sharding import PartitionSpec as P

EXPERTS = 64
CAP = 14


NORM_EPS = 1e-06
LOSS_WEIGHT = 0.25


def to_experts(outgoing):
    return lax.all_to_all(outgoing, "expert", split_axis=1, concat_axis=1, tiled=True)


def to_tokens(outgoing):
    return lax.all_to_all(outgoing, "expert", split_axis=1, concat_axis=1, tiled=True)


DP_SWAP = [(0, 1), (1, 0)]


def dp_joined(own, dp_first, axis):
    other = lax.ppermute(own, "dp", DP_SWAP)
    return jnp.where(
        dp_first,
        jnp.concatenate([own, other], axis=axis),
        jnp.concatenate([other, own], axis=axis),
    )


def dp_halves_sent(part, dp_first, axis):
    half = part.shape[axis] // 2
    low = lax.slice_in_dim(part, 0, half, axis=axis).astype(jnp.bfloat16)
    high = lax.slice_in_dim(part, half, 2 * half, axis=axis).astype(jnp.bfloat16)
    kept = jnp.where(dp_first, low, high)
    arrived = lax.ppermute(jnp.where(dp_first, high, low), "dp", DP_SWAP)
    return kept, arrived


def halves_added(kept, arrived):
    return (kept.astype(jnp.float32) + arrived.astype(jnp.float32)).astype(jnp.bfloat16)


def weight_terms(arrived, activation, grad_in, d_gate_pre, d_up_pre):
    down_part = jnp.einsum(
        "escf,escd->efd", activation, grad_in, preferred_element_type=jnp.float32
    )
    gate_part = jnp.einsum(
        "escd,escf->edf", arrived, d_gate_pre, preferred_element_type=jnp.float32
    )
    up_part = jnp.einsum("escd,escf->edf", arrived, d_up_pre, preferred_element_type=jnp.float32)
    return (jnp.stack([gate_part, up_part], axis=1), down_part)


def per_device(
    context, residual, wo_rows, norm_gain, analyzer_out, gate_probs, expert_ids, w_gate_up, w_down
):
    tok_count, top_count = expert_ids.shape
    feature_count = residual.shape[1]
    tensor_count = lax.axis_size("tensor")
    expert_ranks = lax.axis_size("expert")
    col_count = feature_count // tensor_count
    col_start = lax.axis_index("tensor") * col_count
    local_experts = w_gate_up.shape[0]
    slot_count = EXPERTS * CAP
    expert_range = jnp.arange(EXPERTS, dtype=jnp.int32)
    slot_order = expert_range % local_experts * expert_ranks + expert_range // local_experts
    dp_first = lax.axis_index("dp") == 0
    gate_up_full, down_full = (
        dp_joined(w_gate_up, dp_first, 2),
        dp_joined(w_down, dp_first, 2),
    )
    partial_attn = jnp.dot(context, wo_rows, preferred_element_type=jnp.float32)
    attn_cols = lax.psum_scatter(
        partial_attn.astype(jnp.bfloat16), "tensor", scatter_dimension=1, tiled=True
    )
    hidden_cols = lax.dynamic_slice_in_dim(residual, col_start, col_count, 1).astype(
        jnp.float32
    ) + attn_cols.astype(jnp.float32)
    square_sum = lax.psum(jnp.sum(hidden_cols * hidden_cols, axis=1, keepdims=True), "tensor")
    inv_rms = lax.rsqrt(square_sum / feature_count + NORM_EPS)
    gain_cols = lax.dynamic_slice_in_dim(norm_gain, col_start, col_count, 0)
    normed = (gain_cols * hidden_cols * inv_rms).astype(jnp.bfloat16)
    flat_ids = expert_ids.reshape(-1)
    onehot = (flat_ids[:, None] == expert_range[None, :]).astype(jnp.int32)
    slot_index = jnp.sum((jnp.cumsum(onehot, axis=0) - onehot) * onehot, axis=1)
    expert_slot = jnp.sum(onehot * slot_order[None, :], axis=1)
    dest_row = expert_slot * CAP + slot_index
    sentinel = tok_count * top_count
    row_entry = (
        jnp.full((slot_count,), sentinel, jnp.int32)
        .at[dest_row]
        .set(jnp.arange(sentinel, dtype=jnp.int32))
    )
    row_token = row_entry // top_count
    gate_pad = jnp.concatenate([gate_probs.reshape(-1), jnp.zeros((1,), jnp.float32)])
    row_gate = gate_pad[row_entry]
    normed_pad = jnp.concatenate([normed, jnp.zeros((1, col_count), jnp.bfloat16)], axis=0)
    outgoing = normed_pad[row_token].reshape(local_experts, expert_ranks, CAP, col_count)
    arrived = lax.all_gather(to_experts(outgoing), "tensor", axis=3, tiled=True)
    gate_full = gate_up_full[:, 0]
    up_full = gate_up_full[:, 1]
    pre_gate = jnp.einsum("escd,edf->escf", arrived, gate_full, preferred_element_type=jnp.float32)
    pre_up = jnp.einsum("escd,edf->escf", arrived, up_full, preferred_element_type=jnp.float32)
    activation = (jax.nn.silu(pre_gate) * pre_up).astype(jnp.bfloat16)
    partial_out = jnp.einsum(
        "escf,efd->escd", activation, down_full, preferred_element_type=jnp.float32
    )
    summed_out = lax.psum_scatter(
        partial_out.astype(jnp.bfloat16), "tensor", scatter_dimension=3, tiled=True
    )
    returned = to_tokens(summed_out).reshape(slot_count, col_count)
    entry_out = returned[dest_row].reshape(tok_count, top_count, col_count).astype(jnp.float32)
    block_out = (hidden_cols + jnp.sum(gate_probs[:, :, None] * entry_out, axis=1)).astype(
        jnp.bfloat16
    )
    error = (
        LOSS_WEIGHT * (block_out.astype(jnp.float32) - analyzer_out.astype(jnp.float32))
    ).astype(jnp.bfloat16)
    gate_partial = jnp.sum(error.astype(jnp.float32)[:, None, :] * entry_out, axis=2)
    error_pad = jnp.concatenate([error, jnp.zeros((1, col_count), jnp.bfloat16)], axis=0)
    grad_slot = (row_gate[:, None] * error_pad[row_token].astype(jnp.float32)).astype(jnp.bfloat16)
    grad_slot = grad_slot.reshape(local_experts, expert_ranks, CAP, col_count)
    grad_in = lax.all_gather(to_experts(grad_slot), "tensor", axis=3, tiled=True)
    d_act = jnp.einsum("escd,efd->escf", grad_in, down_full, preferred_element_type=jnp.float32)
    sigmoid_pre = jax.nn.sigmoid(pre_gate)
    d_gate_pre = (d_act * pre_up * sigmoid_pre * (1.0 + pre_gate * (1.0 - sigmoid_pre))).astype(
        jnp.bfloat16
    )
    d_up_pre = (d_act * pre_gate * sigmoid_pre).astype(jnp.bfloat16)
    d_entry_part = jnp.einsum(
        "escf,edf->escd", d_gate_pre, gate_full, preferred_element_type=jnp.float32
    )
    d_entry_part = d_entry_part + jnp.einsum(
        "escf,edf->escd", d_up_pre, up_full, preferred_element_type=jnp.float32
    )
    d_entry_sum = lax.psum_scatter(
        d_entry_part.astype(jnp.bfloat16), "tensor", scatter_dimension=3, tiled=True
    )
    d_returned = to_tokens(d_entry_sum).reshape(slot_count, col_count)
    d_normed = jnp.sum(
        d_returned[dest_row].reshape(tok_count, top_count, col_count).astype(jnp.float32), axis=1
    )
    scaled = gain_cols * d_normed
    norm_partial = jnp.sum(scaled * hidden_cols, axis=1)
    norm_dots, gate_prob_grad = lax.psum((norm_partial, gate_partial), "tensor")
    cubed = inv_rms * inv_rms * inv_rms
    d_hidden = (
        error.astype(jnp.float32)
        + inv_rms * scaled
        - hidden_cols * cubed * norm_dots[:, None] / feature_count
    ).astype(jnp.bfloat16)
    context_grad = lax.dot_general(
        lax.all_gather(d_hidden, "tensor", axis=1, tiled=True),
        wo_rows,
        (((1,), (1,)), ((), ())),
        preferred_element_type=jnp.float32,
    ).astype(jnp.bfloat16)
    gate_up_part, down_part = weight_terms(arrived, activation, grad_in, d_gate_pre, d_up_pre)
    gate_up_kept, gate_up_arrived = dp_halves_sent(gate_up_part, dp_first, 2)
    down_kept, down_arrived = dp_halves_sent(down_part, dp_first, 2)
    gate_up_arrived, down_arrived, context_grad = lax.optimization_barrier(
        (gate_up_arrived, down_arrived, context_grad)
    )
    return (
        block_out,
        context_grad,
        gate_prob_grad,
        halves_added(gate_up_kept, gate_up_arrived),
        halves_added(down_kept, down_arrived),
    )


def solution(mesh):
    in_specs = (
        P(("dp", "expert"), "tensor"),
        P(("dp", "expert"), None),
        P("tensor", None),
        P(),
        P(("dp", "expert"), "tensor"),
        P(("dp", "expert"), None),
        P(("dp", "expert"), None),
        P("expert", None, "dp", "tensor"),
        P("expert", "tensor", "dp"),
    )
    out_specs = (
        P(("dp", "expert"), "tensor"),
        P(("dp", "expert"), "tensor"),
        P(("dp", "expert"), None),
        P("expert", None, "dp", "tensor"),
        P("expert", "tensor", "dp"),
    )
    return jax.shard_map(
        per_device, mesh=mesh, in_specs=in_specs, out_specs=out_specs, check_vma=False
    )
```

```python
import jax
import jax.numpy as jnp
from jax import lax
from jax.sharding import PartitionSpec as P

EXPERTS = 64
CAP = 14


NORM_EPS = 1e-06
LOSS_WEIGHT = 0.25


def to_experts(outgoing):
    return lax.all_to_all(outgoing, "expert", split_axis=1, concat_axis=1, tiled=True)


def to_tokens(outgoing):
    return lax.all_to_all(outgoing, "expert", split_axis=1, concat_axis=1, tiled=True)


DP_SWAP = [(0, 1), (1, 0)]


def tensor_shift(value, shift, count):
    return lax.ppermute(value, "tensor", [(j, (j + shift) % count) for j in range(count)])


def by_source(received, count):
    order = (lax.axis_index("tensor") - jnp.arange(count)) % count
    return jnp.take(jnp.stack(received), order, axis=0)


def tensor_pieces(value):
    count = lax.axis_size("tensor")
    received = [value] + [tensor_shift(value, shift, count) for shift in range(1, count)]
    return by_source(received, count)


def tensor_total(value):
    pieces = tensor_pieces(value)
    total = pieces[0]
    for member in range(1, pieces.shape[0]):
        total = total + pieces[member]
    return total


def tensor_joined(value):
    pieces = tensor_pieces(value)
    return jnp.concatenate([pieces[member] for member in range(pieces.shape[0])], axis=1)


def tensor_scattered(value):
    count = lax.axis_size("tensor")
    width = value.shape[1] // count
    me = lax.axis_index("tensor")
    received = [lax.dynamic_slice_in_dim(value, me * width, width, 1)]
    for shift in range(1, count):
        sent = lax.dynamic_slice_in_dim(value, (me + shift) % count * width, width, 1)
        received.append(tensor_shift(sent, shift, count))
    pieces = by_source(received, count).astype(jnp.float32)
    total = pieces[0]
    for member in range(1, count):
        total = total + pieces[member]
    return total


def dp_joined(own, dp_first, axis):
    other = lax.ppermute(own, "dp", DP_SWAP)
    return jnp.where(
        dp_first,
        jnp.concatenate([own, other], axis=axis),
        jnp.concatenate([other, own], axis=axis),
    )


def dp_halves_sent(part, dp_first, axis):
    half = part.shape[axis] // 2
    low = lax.slice_in_dim(part, 0, half, axis=axis).astype(jnp.bfloat16)
    high = lax.slice_in_dim(part, half, 2 * half, axis=axis).astype(jnp.bfloat16)
    kept = jnp.where(dp_first, low, high)
    arrived = lax.ppermute(jnp.where(dp_first, high, low), "dp", DP_SWAP)
    return kept, arrived


def halves_added(kept, arrived):
    return (kept.astype(jnp.float32) + arrived.astype(jnp.float32)).astype(jnp.bfloat16)


def weight_terms(arrived, activation, grad_in, d_gate_pre, d_up_pre):
    down_part = jnp.einsum(
        "escf,escd->efd", activation, grad_in, preferred_element_type=jnp.float32
    )
    gate_part = jnp.einsum(
        "escd,escf->edf", arrived, d_gate_pre, preferred_element_type=jnp.float32
    )
    up_part = jnp.einsum("escd,escf->edf", arrived, d_up_pre, preferred_element_type=jnp.float32)
    return (jnp.stack([gate_part, up_part], axis=1), down_part)


def per_device(
    context, residual, wo_rows, norm_gain, analyzer_out, gate_probs, expert_ids, w_gate_up, w_down
):
    tok_count, top_count = expert_ids.shape
    feature_count = residual.shape[1]
    tensor_count = lax.axis_size("tensor")
    expert_ranks = lax.axis_size("expert")
    col_count = feature_count // tensor_count
    col_start = lax.axis_index("tensor") * col_count
    local_experts = w_gate_up.shape[0]
    slot_count = EXPERTS * CAP
    expert_range = jnp.arange(EXPERTS, dtype=jnp.int32)
    slot_order = expert_range % local_experts * expert_ranks + expert_range // local_experts
    dp_first = lax.axis_index("dp") == 0
    gate_up_full, down_full = (
        dp_joined(w_gate_up, dp_first, 2),
        dp_joined(w_down, dp_first, 2),
    )
    partial_attn = jnp.dot(context, wo_rows, preferred_element_type=jnp.float32)
    attn_cols = tensor_scattered(partial_attn.astype(jnp.bfloat16))
    hidden_cols = lax.dynamic_slice_in_dim(residual, col_start, col_count, 1).astype(
        jnp.float32
    ) + attn_cols
    square_sum = tensor_total(jnp.sum(hidden_cols * hidden_cols, axis=1, keepdims=True))
    inv_rms = lax.rsqrt(square_sum / feature_count + NORM_EPS)
    gain_cols = lax.dynamic_slice_in_dim(norm_gain, col_start, col_count, 0)
    normed = (gain_cols * hidden_cols * inv_rms).astype(jnp.bfloat16)
    flat_ids = expert_ids.reshape(-1)
    onehot = (flat_ids[:, None] == expert_range[None, :]).astype(jnp.int32)
    slot_index = jnp.sum((jnp.cumsum(onehot, axis=0) - onehot) * onehot, axis=1)
    expert_slot = jnp.sum(onehot * slot_order[None, :], axis=1)
    dest_row = expert_slot * CAP + slot_index
    sentinel = tok_count * top_count
    row_entry = (
        jnp.full((slot_count,), sentinel, jnp.int32)
        .at[dest_row]
        .set(jnp.arange(sentinel, dtype=jnp.int32))
    )
    row_token = row_entry // top_count
    gate_pad = jnp.concatenate([gate_probs.reshape(-1), jnp.zeros((1,), jnp.float32)])
    row_gate = gate_pad[row_entry]
    normed_pad = jnp.concatenate([normed, jnp.zeros((1, col_count), jnp.bfloat16)], axis=0)
    outgoing = normed_pad[row_token].reshape(local_experts, expert_ranks, CAP, col_count)
    arrived = lax.all_gather(to_experts(outgoing), "tensor", axis=3, tiled=True)
    gate_full = gate_up_full[:, 0]
    up_full = gate_up_full[:, 1]
    pre_gate = jnp.einsum("escd,edf->escf", arrived, gate_full, preferred_element_type=jnp.float32)
    pre_up = jnp.einsum("escd,edf->escf", arrived, up_full, preferred_element_type=jnp.float32)
    activation = (jax.nn.silu(pre_gate) * pre_up).astype(jnp.bfloat16)
    partial_out = jnp.einsum(
        "escf,efd->escd", activation, down_full, preferred_element_type=jnp.float32
    )
    summed_out = lax.psum_scatter(
        partial_out.astype(jnp.bfloat16), "tensor", scatter_dimension=3, tiled=True
    )
    returned = to_tokens(summed_out).reshape(slot_count, col_count)
    entry_out = returned[dest_row].reshape(tok_count, top_count, col_count).astype(jnp.float32)
    block_out = (hidden_cols + jnp.sum(gate_probs[:, :, None] * entry_out, axis=1)).astype(
        jnp.bfloat16
    )
    error = (
        LOSS_WEIGHT * (block_out.astype(jnp.float32) - analyzer_out.astype(jnp.float32))
    ).astype(jnp.bfloat16)
    gate_partial = jnp.sum(error.astype(jnp.float32)[:, None, :] * entry_out, axis=2)
    error_pad = jnp.concatenate([error, jnp.zeros((1, col_count), jnp.bfloat16)], axis=0)
    grad_slot = (row_gate[:, None] * error_pad[row_token].astype(jnp.float32)).astype(jnp.bfloat16)
    grad_slot = grad_slot.reshape(local_experts, expert_ranks, CAP, col_count)
    grad_in = lax.all_gather(to_experts(grad_slot), "tensor", axis=3, tiled=True)
    d_act = jnp.einsum("escd,efd->escf", grad_in, down_full, preferred_element_type=jnp.float32)
    sigmoid_pre = jax.nn.sigmoid(pre_gate)
    d_gate_pre = (d_act * pre_up * sigmoid_pre * (1.0 + pre_gate * (1.0 - sigmoid_pre))).astype(
        jnp.bfloat16
    )
    d_up_pre = (d_act * pre_gate * sigmoid_pre).astype(jnp.bfloat16)
    d_entry_part = jnp.einsum(
        "escf,edf->escd", d_gate_pre, gate_full, preferred_element_type=jnp.float32
    )
    d_entry_part = d_entry_part + jnp.einsum(
        "escf,edf->escd", d_up_pre, up_full, preferred_element_type=jnp.float32
    )
    d_entry_sum = lax.psum_scatter(
        d_entry_part.astype(jnp.bfloat16), "tensor", scatter_dimension=3, tiled=True
    )
    d_returned = to_tokens(d_entry_sum).reshape(slot_count, col_count)
    d_normed = jnp.sum(
        d_returned[dest_row].reshape(tok_count, top_count, col_count).astype(jnp.float32), axis=1
    )
    scaled = gain_cols * d_normed
    norm_partial = jnp.sum(scaled * hidden_cols, axis=1)
    dots_total = tensor_total(jnp.concatenate([norm_partial[:, None], gate_partial], axis=1))
    norm_dots, gate_prob_grad = dots_total[:, 0], dots_total[:, 1:]
    cubed = inv_rms * inv_rms * inv_rms
    d_hidden = (
        error.astype(jnp.float32)
        + inv_rms * scaled
        - hidden_cols * cubed * norm_dots[:, None] / feature_count
    ).astype(jnp.bfloat16)
    context_grad = lax.dot_general(
        tensor_joined(d_hidden),
        wo_rows,
        (((1,), (1,)), ((), ())),
        preferred_element_type=jnp.float32,
    ).astype(jnp.bfloat16)
    gate_up_part, down_part = weight_terms(arrived, activation, grad_in, d_gate_pre, d_up_pre)
    gate_up_kept, gate_up_arrived = dp_halves_sent(gate_up_part, dp_first, 2)
    down_kept, down_arrived = dp_halves_sent(down_part, dp_first, 2)
    gate_up_arrived, down_arrived, context_grad = lax.optimization_barrier(
        (gate_up_arrived, down_arrived, context_grad)
    )
    return (
        block_out,
        context_grad,
        gate_prob_grad,
        halves_added(gate_up_kept, gate_up_arrived),
        halves_added(down_kept, down_arrived),
    )


def solution(mesh):
    in_specs = (
        P(("dp", "expert"), "tensor"),
        P(("dp", "expert"), None),
        P("tensor", None),
        P(),
        P(("dp", "expert"), "tensor"),
        P(("dp", "expert"), None),
        P(("dp", "expert"), None),
        P("expert", None, "dp", "tensor"),
        P("expert", "tensor", "dp"),
    )
    out_specs = (
        P(("dp", "expert"), "tensor"),
        P(("dp", "expert"), "tensor"),
        P(("dp", "expert"), None),
        P("expert", None, "dp", "tensor"),
        P("expert", "tensor", "dp"),
    )
    return jax.shard_map(
        per_device, mesh=mesh, in_specs=in_specs, out_specs=out_specs, check_vma=False
    )
```

```python
import jax
import jax.numpy as jnp
from jax import lax
from jax.sharding import PartitionSpec as P

EXPERTS = 64
CAP = 14


NORM_EPS = 1e-06
LOSS_WEIGHT = 0.25


def to_experts(outgoing):
    return lax.all_to_all(outgoing, "expert", split_axis=1, concat_axis=1, tiled=True)


def to_tokens(outgoing):
    return lax.all_to_all(outgoing, "expert", split_axis=1, concat_axis=1, tiled=True)


DP_SWAP = [(0, 1), (1, 0)]


def tensor_shift(value, shift, count):
    return lax.ppermute(value, "tensor", [(j, (j + shift) % count) for j in range(count)])


def by_source(received, count):
    order = (lax.axis_index("tensor") - jnp.arange(count)) % count
    return jnp.take(jnp.stack(received), order, axis=0)


def tensor_pieces(value):
    count = lax.axis_size("tensor")
    received = [value] + [tensor_shift(value, shift, count) for shift in range(1, count)]
    return by_source(received, count)


def tensor_total(value):
    pieces = tensor_pieces(value)
    total = pieces[0]
    for member in range(1, pieces.shape[0]):
        total = total + pieces[member]
    return total


def tensor_scattered(value):
    count = lax.axis_size("tensor")
    width = value.shape[1] // count
    me = lax.axis_index("tensor")
    received = [lax.dynamic_slice_in_dim(value, me * width, width, 1)]
    for shift in range(1, count):
        sent = lax.dynamic_slice_in_dim(value, (me + shift) % count * width, width, 1)
        received.append(tensor_shift(sent, shift, count))
    pieces = by_source(received, count).astype(jnp.float32)
    total = pieces[0]
    for member in range(1, count):
        total = total + pieces[member]
    return total


def dp_joined(own, dp_first, axis):
    other = lax.ppermute(own, "dp", DP_SWAP)
    return jnp.where(
        dp_first,
        jnp.concatenate([own, other], axis=axis),
        jnp.concatenate([other, own], axis=axis),
    )


def dp_halves_sent(part, dp_first, axis):
    half = part.shape[axis] // 2
    low = lax.slice_in_dim(part, 0, half, axis=axis).astype(jnp.bfloat16)
    high = lax.slice_in_dim(part, half, 2 * half, axis=axis).astype(jnp.bfloat16)
    kept = jnp.where(dp_first, low, high)
    arrived = lax.ppermute(jnp.where(dp_first, high, low), "dp", DP_SWAP)
    return kept, arrived


def halves_added(kept, arrived):
    return (kept.astype(jnp.float32) + arrived.astype(jnp.float32)).astype(jnp.bfloat16)


def weight_terms(arrived, activation, grad_in, d_gate_pre, d_up_pre):
    down_part = jnp.einsum(
        "escf,escd->efd", activation, grad_in, preferred_element_type=jnp.float32
    )
    gate_part = jnp.einsum(
        "escd,escf->edf", arrived, d_gate_pre, preferred_element_type=jnp.float32
    )
    up_part = jnp.einsum("escd,escf->edf", arrived, d_up_pre, preferred_element_type=jnp.float32)
    return (jnp.stack([gate_part, up_part], axis=1), down_part)


def per_device(
    context, residual, wo_rows, norm_gain, analyzer_out, gate_probs, expert_ids, w_gate_up, w_down
):
    tok_count, top_count = expert_ids.shape
    feature_count = residual.shape[1]
    tensor_count = lax.axis_size("tensor")
    expert_ranks = lax.axis_size("expert")
    col_count = feature_count // tensor_count
    col_start = lax.axis_index("tensor") * col_count
    local_experts = w_gate_up.shape[0]
    slot_count = EXPERTS * CAP
    expert_range = jnp.arange(EXPERTS, dtype=jnp.int32)
    slot_order = expert_range % local_experts * expert_ranks + expert_range // local_experts
    dp_first = lax.axis_index("dp") == 0
    gate_up_full, down_full = (
        dp_joined(w_gate_up, dp_first, 2),
        dp_joined(w_down, dp_first, 2),
    )
    partial_attn = jnp.dot(context, wo_rows, preferred_element_type=jnp.float32)
    attn_cols = tensor_scattered(partial_attn.astype(jnp.bfloat16))
    hidden_cols = lax.dynamic_slice_in_dim(residual, col_start, col_count, 1).astype(
        jnp.float32
    ) + attn_cols
    square_sum = tensor_total(jnp.sum(hidden_cols * hidden_cols, axis=1, keepdims=True))
    inv_rms = lax.rsqrt(square_sum / feature_count + NORM_EPS)
    gain_cols = lax.dynamic_slice_in_dim(norm_gain, col_start, col_count, 0)
    normed = (gain_cols * hidden_cols * inv_rms).astype(jnp.bfloat16)
    flat_ids = expert_ids.reshape(-1)
    onehot = (flat_ids[:, None] == expert_range[None, :]).astype(jnp.int32)
    slot_index = jnp.sum((jnp.cumsum(onehot, axis=0) - onehot) * onehot, axis=1)
    expert_slot = jnp.sum(onehot * slot_order[None, :], axis=1)
    dest_row = expert_slot * CAP + slot_index
    sentinel = tok_count * top_count
    row_entry = (
        jnp.full((slot_count,), sentinel, jnp.int32)
        .at[dest_row]
        .set(jnp.arange(sentinel, dtype=jnp.int32))
    )
    row_token = row_entry // top_count
    gate_pad = jnp.concatenate([gate_probs.reshape(-1), jnp.zeros((1,), jnp.float32)])
    row_gate = gate_pad[row_entry]
    normed_pad = jnp.concatenate([normed, jnp.zeros((1, col_count), jnp.bfloat16)], axis=0)
    outgoing = normed_pad[row_token].reshape(local_experts, expert_ranks, CAP, col_count)
    arrived = lax.all_gather(to_experts(outgoing), "tensor", axis=3, tiled=True)
    gate_full = gate_up_full[:, 0]
    up_full = gate_up_full[:, 1]
    pre_gate = jnp.einsum("escd,edf->escf", arrived, gate_full, preferred_element_type=jnp.float32)
    pre_up = jnp.einsum("escd,edf->escf", arrived, up_full, preferred_element_type=jnp.float32)
    activation = (jax.nn.silu(pre_gate) * pre_up).astype(jnp.bfloat16)
    partial_out = jnp.einsum(
        "escf,efd->escd", activation, down_full, preferred_element_type=jnp.float32
    )
    summed_out = lax.psum_scatter(
        partial_out.astype(jnp.bfloat16), "tensor", scatter_dimension=3, tiled=True
    )
    returned = to_tokens(summed_out).reshape(slot_count, col_count)
    entry_out = returned[dest_row].reshape(tok_count, top_count, col_count).astype(jnp.float32)
    block_out = (hidden_cols + jnp.sum(gate_probs[:, :, None] * entry_out, axis=1)).astype(
        jnp.bfloat16
    )
    error = (
        LOSS_WEIGHT * (block_out.astype(jnp.float32) - analyzer_out.astype(jnp.float32))
    ).astype(jnp.bfloat16)
    gate_partial = jnp.sum(error.astype(jnp.float32)[:, None, :] * entry_out, axis=2)
    error_pad = jnp.concatenate([error, jnp.zeros((1, col_count), jnp.bfloat16)], axis=0)
    grad_slot = (row_gate[:, None] * error_pad[row_token].astype(jnp.float32)).astype(jnp.bfloat16)
    grad_slot = grad_slot.reshape(local_experts, expert_ranks, CAP, col_count)
    grad_in = lax.all_gather(to_experts(grad_slot), "tensor", axis=3, tiled=True)
    d_act = jnp.einsum("escd,efd->escf", grad_in, down_full, preferred_element_type=jnp.float32)
    sigmoid_pre = jax.nn.sigmoid(pre_gate)
    d_gate_pre = (d_act * pre_up * sigmoid_pre * (1.0 + pre_gate * (1.0 - sigmoid_pre))).astype(
        jnp.bfloat16
    )
    d_up_pre = (d_act * pre_gate * sigmoid_pre).astype(jnp.bfloat16)
    d_entry_part = jnp.einsum(
        "escf,edf->escd", d_gate_pre, gate_full, preferred_element_type=jnp.float32
    )
    d_entry_part = d_entry_part + jnp.einsum(
        "escf,edf->escd", d_up_pre, up_full, preferred_element_type=jnp.float32
    )
    d_entry_sum = lax.psum_scatter(
        d_entry_part.astype(jnp.bfloat16), "tensor", scatter_dimension=3, tiled=True
    )
    d_returned = to_tokens(d_entry_sum).reshape(slot_count, col_count)
    d_normed = jnp.sum(
        d_returned[dest_row].reshape(tok_count, top_count, col_count).astype(jnp.float32), axis=1
    )
    scaled = gain_cols * d_normed
    norm_partial = jnp.sum(scaled * hidden_cols, axis=1)
    norm_dots, gate_prob_grad = lax.psum((norm_partial, gate_partial), "tensor")
    cubed = inv_rms * inv_rms * inv_rms
    d_hidden = (
        error.astype(jnp.float32)
        + inv_rms * scaled
        - hidden_cols * cubed * norm_dots[:, None] / feature_count
    ).astype(jnp.bfloat16)
    context_grad = lax.dot_general(
        lax.all_gather(d_hidden, "tensor", axis=1, tiled=True),
        wo_rows,
        (((1,), (1,)), ((), ())),
        preferred_element_type=jnp.float32,
    ).astype(jnp.bfloat16)
    gate_up_part, down_part = weight_terms(arrived, activation, grad_in, d_gate_pre, d_up_pre)
    gate_up_kept, gate_up_arrived = dp_halves_sent(gate_up_part, dp_first, 2)
    down_kept, down_arrived = dp_halves_sent(down_part, dp_first, 2)
    gate_up_arrived, down_arrived, context_grad = lax.optimization_barrier(
        (gate_up_arrived, down_arrived, context_grad)
    )
    return (
        block_out,
        context_grad,
        gate_prob_grad,
        halves_added(gate_up_kept, gate_up_arrived),
        halves_added(down_kept, down_arrived),
    )


def solution(mesh):
    in_specs = (
        P(("dp", "expert"), "tensor"),
        P(("dp", "expert"), None),
        P("tensor", None),
        P(),
        P(("dp", "expert"), "tensor"),
        P(("dp", "expert"), None),
        P(("dp", "expert"), None),
        P("expert", None, "dp", "tensor"),
        P("expert", "tensor", "dp"),
    )
    out_specs = (
        P(("dp", "expert"), "tensor"),
        P(("dp", "expert"), "tensor"),
        P(("dp", "expert"), None),
        P("expert", None, "dp", "tensor"),
        P("expert", "tensor", "dp"),
    )
    return jax.shard_map(
        per_device, mesh=mesh, in_specs=in_specs, out_specs=out_specs, check_vma=False
    )
```

```python
import jax
import jax.numpy as jnp
from jax import lax
from jax.sharding import PartitionSpec as P

EXPERTS = 64
CAP = 14


NORM_EPS = 1e-06
LOSS_WEIGHT = 0.25


def to_experts(outgoing):
    return lax.all_to_all(outgoing, "expert", split_axis=1, concat_axis=1, tiled=True)


def to_tokens(outgoing):
    return lax.all_to_all(outgoing, "expert", split_axis=1, concat_axis=1, tiled=True)


DP_SWAP = [(0, 1), (1, 0)]


def tensor_shift(value, shift, count):
    return lax.ppermute(value, "tensor", [(j, (j + shift) % count) for j in range(count)])


def by_source(received, count):
    order = (lax.axis_index("tensor") - jnp.arange(count)) % count
    return jnp.take(jnp.stack(received), order, axis=0)


def tensor_pieces(value):
    count = lax.axis_size("tensor")
    received = [value] + [tensor_shift(value, shift, count) for shift in range(1, count)]
    return by_source(received, count)


def tensor_total(value):
    pieces = tensor_pieces(value)
    total = pieces[0]
    for member in range(1, pieces.shape[0]):
        total = total + pieces[member]
    return total


def tensor_scattered(value):
    count = lax.axis_size("tensor")
    width = value.shape[1] // count
    me = lax.axis_index("tensor")
    received = [lax.dynamic_slice_in_dim(value, me * width, width, 1)]
    for shift in range(1, count):
        sent = lax.dynamic_slice_in_dim(value, (me + shift) % count * width, width, 1)
        received.append(tensor_shift(sent, shift, count))
    pieces = by_source(received, count).astype(jnp.float32)
    total = pieces[0]
    for member in range(1, count):
        total = total + pieces[member]
    return total


def dp_joined(own, dp_first, axis):
    other = lax.ppermute(own, "dp", DP_SWAP)
    return jnp.where(
        dp_first,
        jnp.concatenate([own, other], axis=axis),
        jnp.concatenate([other, own], axis=axis),
    )


def dp_halves_sent(part, dp_first, axis):
    half = part.shape[axis] // 2
    low = lax.slice_in_dim(part, 0, half, axis=axis).astype(jnp.bfloat16)
    high = lax.slice_in_dim(part, half, 2 * half, axis=axis).astype(jnp.bfloat16)
    kept = jnp.where(dp_first, low, high)
    arrived = lax.ppermute(jnp.where(dp_first, high, low), "dp", DP_SWAP)
    return kept, arrived


def halves_added(kept, arrived):
    return (kept.astype(jnp.float32) + arrived.astype(jnp.float32)).astype(jnp.bfloat16)


def weight_terms(arrived, activation, grad_in, d_gate_pre, d_up_pre):
    down_part = jnp.einsum(
        "escf,escd->efd", activation, grad_in, preferred_element_type=jnp.float32
    )
    gate_part = jnp.einsum(
        "escd,escf->edf", arrived, d_gate_pre, preferred_element_type=jnp.float32
    )
    up_part = jnp.einsum("escd,escf->edf", arrived, d_up_pre, preferred_element_type=jnp.float32)
    return (jnp.stack([gate_part, up_part], axis=1), down_part)


def per_device(
    context, residual, wo_rows, norm_gain, analyzer_out, gate_probs, expert_ids, w_gate_up, w_down
):
    tok_count, top_count = expert_ids.shape
    feature_count = residual.shape[1]
    tensor_count = lax.axis_size("tensor")
    expert_ranks = lax.axis_size("expert")
    col_count = feature_count // tensor_count
    col_start = lax.axis_index("tensor") * col_count
    local_experts = w_gate_up.shape[0]
    slot_count = EXPERTS * CAP
    expert_range = jnp.arange(EXPERTS, dtype=jnp.int32)
    slot_order = expert_range % local_experts * expert_ranks + expert_range // local_experts
    dp_first = lax.axis_index("dp") == 0
    down_other = lax.ppermute(w_down, "dp", DP_SWAP)
    partial_attn = jnp.dot(context, wo_rows, preferred_element_type=jnp.float32)
    attn_cols = tensor_scattered(partial_attn.astype(jnp.bfloat16))
    hidden_cols = lax.dynamic_slice_in_dim(residual, col_start, col_count, 1).astype(
        jnp.float32
    ) + attn_cols
    square_sum = tensor_total(jnp.sum(hidden_cols * hidden_cols, axis=1, keepdims=True))
    inv_rms = lax.rsqrt(square_sum / feature_count + NORM_EPS)
    gain_cols = lax.dynamic_slice_in_dim(norm_gain, col_start, col_count, 0)
    normed = (gain_cols * hidden_cols * inv_rms).astype(jnp.bfloat16)
    flat_ids = expert_ids.reshape(-1)
    onehot = (flat_ids[:, None] == expert_range[None, :]).astype(jnp.int32)
    slot_index = jnp.sum((jnp.cumsum(onehot, axis=0) - onehot) * onehot, axis=1)
    expert_slot = jnp.sum(onehot * slot_order[None, :], axis=1)
    dest_row = expert_slot * CAP + slot_index
    sentinel = tok_count * top_count
    row_entry = (
        jnp.full((slot_count,), sentinel, jnp.int32)
        .at[dest_row]
        .set(jnp.arange(sentinel, dtype=jnp.int32))
    )
    row_token = row_entry // top_count
    gate_pad = jnp.concatenate([gate_probs.reshape(-1), jnp.zeros((1,), jnp.float32)])
    row_gate = gate_pad[row_entry]
    normed_pad = jnp.concatenate([normed, jnp.zeros((1, col_count), jnp.bfloat16)], axis=0)
    outgoing = normed_pad[row_token].reshape(local_experts, expert_ranks, CAP, col_count)
    down_other, outgoing = lax.optimization_barrier((down_other, outgoing))
    gate_up_full = dp_joined(w_gate_up, dp_first, 2)
    down_full = jnp.where(
        dp_first,
        jnp.concatenate([w_down, down_other], axis=2),
        jnp.concatenate([down_other, w_down], axis=2),
    )
    arrived = lax.all_gather(to_experts(outgoing), "tensor", axis=3, tiled=True)
    gate_full = gate_up_full[:, 0]
    up_full = gate_up_full[:, 1]
    pre_gate = jnp.einsum("escd,edf->escf", arrived, gate_full, preferred_element_type=jnp.float32)
    pre_up = jnp.einsum("escd,edf->escf", arrived, up_full, preferred_element_type=jnp.float32)
    activation = (jax.nn.silu(pre_gate) * pre_up).astype(jnp.bfloat16)
    partial_out = jnp.einsum(
        "escf,efd->escd", activation, down_full, preferred_element_type=jnp.float32
    )
    summed_out = lax.psum_scatter(
        partial_out.astype(jnp.bfloat16), "tensor", scatter_dimension=3, tiled=True
    )
    returned = to_tokens(summed_out).reshape(slot_count, col_count)
    entry_out = returned[dest_row].reshape(tok_count, top_count, col_count).astype(jnp.float32)
    block_out = (hidden_cols + jnp.sum(gate_probs[:, :, None] * entry_out, axis=1)).astype(
        jnp.bfloat16
    )
    error = (
        LOSS_WEIGHT * (block_out.astype(jnp.float32) - analyzer_out.astype(jnp.float32))
    ).astype(jnp.bfloat16)
    gate_partial = jnp.sum(error.astype(jnp.float32)[:, None, :] * entry_out, axis=2)
    error_pad = jnp.concatenate([error, jnp.zeros((1, col_count), jnp.bfloat16)], axis=0)
    grad_slot = (row_gate[:, None] * error_pad[row_token].astype(jnp.float32)).astype(jnp.bfloat16)
    grad_slot = grad_slot.reshape(local_experts, expert_ranks, CAP, col_count)
    grad_in = lax.all_gather(to_experts(grad_slot), "tensor", axis=3, tiled=True)
    d_act = jnp.einsum("escd,efd->escf", grad_in, down_full, preferred_element_type=jnp.float32)
    sigmoid_pre = jax.nn.sigmoid(pre_gate)
    d_gate_pre = (d_act * pre_up * sigmoid_pre * (1.0 + pre_gate * (1.0 - sigmoid_pre))).astype(
        jnp.bfloat16
    )
    d_up_pre = (d_act * pre_gate * sigmoid_pre).astype(jnp.bfloat16)
    d_entry_part = jnp.einsum(
        "escf,edf->escd", d_gate_pre, gate_full, preferred_element_type=jnp.float32
    )
    d_entry_part = d_entry_part + jnp.einsum(
        "escf,edf->escd", d_up_pre, up_full, preferred_element_type=jnp.float32
    )
    d_entry_sum = lax.psum_scatter(
        d_entry_part.astype(jnp.bfloat16), "tensor", scatter_dimension=3, tiled=True
    )
    d_returned = to_tokens(d_entry_sum).reshape(slot_count, col_count)
    d_normed = jnp.sum(
        d_returned[dest_row].reshape(tok_count, top_count, col_count).astype(jnp.float32), axis=1
    )
    scaled = gain_cols * d_normed
    norm_partial = jnp.sum(scaled * hidden_cols, axis=1)
    norm_dots, gate_prob_grad = lax.psum((norm_partial, gate_partial), "tensor")
    cubed = inv_rms * inv_rms * inv_rms
    d_hidden = (
        error.astype(jnp.float32)
        + inv_rms * scaled
        - hidden_cols * cubed * norm_dots[:, None] / feature_count
    ).astype(jnp.bfloat16)
    context_grad = lax.dot_general(
        lax.all_gather(d_hidden, "tensor", axis=1, tiled=True),
        wo_rows,
        (((1,), (1,)), ((), ())),
        preferred_element_type=jnp.float32,
    ).astype(jnp.bfloat16)
    gate_up_part, down_part = weight_terms(arrived, activation, grad_in, d_gate_pre, d_up_pre)
    gate_up_kept, gate_up_arrived = dp_halves_sent(gate_up_part, dp_first, 2)
    down_kept, down_arrived = dp_halves_sent(down_part, dp_first, 2)
    gate_up_arrived, down_arrived, context_grad = lax.optimization_barrier(
        (gate_up_arrived, down_arrived, context_grad)
    )
    return (
        block_out,
        context_grad,
        gate_prob_grad,
        halves_added(gate_up_kept, gate_up_arrived),
        halves_added(down_kept, down_arrived),
    )


def solution(mesh):
    in_specs = (
        P(("dp", "expert"), "tensor"),
        P(("dp", "expert"), None),
        P("tensor", None),
        P(),
        P(("dp", "expert"), "tensor"),
        P(("dp", "expert"), None),
        P(("dp", "expert"), None),
        P("expert", None, "dp", "tensor"),
        P("expert", "tensor", "dp"),
    )
    out_specs = (
        P(("dp", "expert"), "tensor"),
        P(("dp", "expert"), "tensor"),
        P(("dp", "expert"), None),
        P("expert", None, "dp", "tensor"),
        P("expert", "tensor", "dp"),
    )
    return jax.shard_map(
        per_device, mesh=mesh, in_specs=in_specs, out_specs=out_specs, check_vma=False
    )
```

```python
import jax
import jax.numpy as jnp
from jax import lax
from jax.sharding import PartitionSpec as P

EXPERTS = 64
CAP = 14


NORM_EPS = 1e-06
LOSS_WEIGHT = 0.25


def to_experts(outgoing):
    return lax.all_to_all(outgoing, "expert", split_axis=1, concat_axis=1, tiled=True)


def to_tokens(outgoing):
    return lax.all_to_all(outgoing, "expert", split_axis=1, concat_axis=1, tiled=True)


DP_SWAP = [(0, 1), (1, 0)]


def tensor_shift(value, shift, count):
    return lax.ppermute(value, "tensor", [(j, (j + shift) % count) for j in range(count)])


def by_source(received, count):
    order = (lax.axis_index("tensor") - jnp.arange(count)) % count
    return jnp.take(jnp.stack(received), order, axis=0)


def tensor_pieces(value):
    count = lax.axis_size("tensor")
    received = [value] + [tensor_shift(value, shift, count) for shift in range(1, count)]
    return by_source(received, count)


def tensor_total(value):
    pieces = tensor_pieces(value)
    total = pieces[0]
    for member in range(1, pieces.shape[0]):
        total = total + pieces[member]
    return total


def tensor_scattered(value):
    count = lax.axis_size("tensor")
    width = value.shape[1] // count
    me = lax.axis_index("tensor")
    received = [lax.dynamic_slice_in_dim(value, me * width, width, 1)]
    for shift in range(1, count):
        sent = lax.dynamic_slice_in_dim(value, (me + shift) % count * width, width, 1)
        received.append(tensor_shift(sent, shift, count))
    pieces = by_source(received, count).astype(jnp.float32)
    total = pieces[0]
    for member in range(1, count):
        total = total + pieces[member]
    return total


def dp_joined(own, dp_first, axis):
    other = lax.ppermute(own, "dp", DP_SWAP)
    return jnp.where(
        dp_first,
        jnp.concatenate([own, other], axis=axis),
        jnp.concatenate([other, own], axis=axis),
    )


def dp_halves_sent(part, dp_first, axis):
    half = part.shape[axis] // 2
    low = lax.slice_in_dim(part, 0, half, axis=axis).astype(jnp.bfloat16)
    high = lax.slice_in_dim(part, half, 2 * half, axis=axis).astype(jnp.bfloat16)
    kept = jnp.where(dp_first, low, high)
    arrived = lax.ppermute(jnp.where(dp_first, high, low), "dp", DP_SWAP)
    return kept, arrived


def halves_added(kept, arrived):
    return (kept.astype(jnp.float32) + arrived.astype(jnp.float32)).astype(jnp.bfloat16)


def weight_terms(arrived, activation, grad_in, d_gate_pre, d_up_pre):
    down_part = jnp.einsum(
        "escf,escd->efd", activation, grad_in, preferred_element_type=jnp.float32
    )
    gate_part = jnp.einsum(
        "escd,escf->edf", arrived, d_gate_pre, preferred_element_type=jnp.float32
    )
    up_part = jnp.einsum("escd,escf->edf", arrived, d_up_pre, preferred_element_type=jnp.float32)
    return (jnp.stack([gate_part, up_part], axis=1), down_part)


def per_device(
    context, residual, wo_rows, norm_gain, analyzer_out, gate_probs, expert_ids, w_gate_up, w_down
):
    tok_count, top_count = expert_ids.shape
    feature_count = residual.shape[1]
    tensor_count = lax.axis_size("tensor")
    expert_ranks = lax.axis_size("expert")
    col_count = feature_count // tensor_count
    col_start = lax.axis_index("tensor") * col_count
    local_experts = w_gate_up.shape[0]
    slot_count = EXPERTS * CAP
    expert_range = jnp.arange(EXPERTS, dtype=jnp.int32)
    slot_order = expert_range % local_experts * expert_ranks + expert_range // local_experts
    dp_first = lax.axis_index("dp") == 0
    down_other = lax.ppermute(w_down, "dp", DP_SWAP)
    partial_attn = jnp.dot(context, wo_rows, preferred_element_type=jnp.float32)
    attn_cols = tensor_scattered(partial_attn.astype(jnp.bfloat16))
    hidden_cols = lax.dynamic_slice_in_dim(residual, col_start, col_count, 1).astype(
        jnp.float32
    ) + attn_cols
    square_sum = tensor_total(jnp.sum(hidden_cols * hidden_cols, axis=1, keepdims=True))
    inv_rms = lax.rsqrt(square_sum / feature_count + NORM_EPS)
    gain_cols = lax.dynamic_slice_in_dim(norm_gain, col_start, col_count, 0)
    normed = (gain_cols * hidden_cols * inv_rms).astype(jnp.bfloat16)
    flat_ids = expert_ids.reshape(-1)
    onehot = (flat_ids[:, None] == expert_range[None, :]).astype(jnp.int32)
    slot_index = jnp.sum((jnp.cumsum(onehot, axis=0) - onehot) * onehot, axis=1)
    expert_slot = jnp.sum(onehot * slot_order[None, :], axis=1)
    dest_row = expert_slot * CAP + slot_index
    sentinel = tok_count * top_count
    row_entry = (
        jnp.full((slot_count,), sentinel, jnp.int32)
        .at[dest_row]
        .set(jnp.arange(sentinel, dtype=jnp.int32))
    )
    row_token = row_entry // top_count
    gate_pad = jnp.concatenate([gate_probs.reshape(-1), jnp.zeros((1,), jnp.float32)])
    row_gate = gate_pad[row_entry]
    normed_pad = jnp.concatenate([normed, jnp.zeros((1, col_count), jnp.bfloat16)], axis=0)
    outgoing = normed_pad[row_token].reshape(local_experts, expert_ranks, CAP, col_count)
    first_other = lax.ppermute(w_gate_up[0:1, 0:1], "dp", DP_SWAP)
    down_other, first_other, outgoing = lax.optimization_barrier(
        (down_other, first_other, outgoing)
    )
    second_other = lax.ppermute(w_gate_up[0:1, 1:2], "dp", DP_SWAP)
    rest_other = lax.ppermute(w_gate_up[1:], "dp", DP_SWAP)
    gate_up_other = jnp.concatenate(
        [jnp.concatenate([first_other, second_other], axis=1), rest_other], axis=0
    )
    gate_up_full = jnp.where(
        dp_first,
        jnp.concatenate([w_gate_up, gate_up_other], axis=2),
        jnp.concatenate([gate_up_other, w_gate_up], axis=2),
    )
    down_full = jnp.where(
        dp_first,
        jnp.concatenate([w_down, down_other], axis=2),
        jnp.concatenate([down_other, w_down], axis=2),
    )
    arrived = lax.all_gather(to_experts(outgoing), "tensor", axis=3, tiled=True)
    gate_full = gate_up_full[:, 0]
    up_full = gate_up_full[:, 1]
    pre_gate = jnp.einsum("escd,edf->escf", arrived, gate_full, preferred_element_type=jnp.float32)
    pre_up = jnp.einsum("escd,edf->escf", arrived, up_full, preferred_element_type=jnp.float32)
    activation = (jax.nn.silu(pre_gate) * pre_up).astype(jnp.bfloat16)
    partial_out = jnp.einsum(
        "escf,efd->escd", activation, down_full, preferred_element_type=jnp.float32
    )
    summed_out = lax.psum_scatter(
        partial_out.astype(jnp.bfloat16), "tensor", scatter_dimension=3, tiled=True
    )
    returned = to_tokens(summed_out).reshape(slot_count, col_count)
    entry_out = returned[dest_row].reshape(tok_count, top_count, col_count).astype(jnp.float32)
    block_out = (hidden_cols + jnp.sum(gate_probs[:, :, None] * entry_out, axis=1)).astype(
        jnp.bfloat16
    )
    error = (
        LOSS_WEIGHT * (block_out.astype(jnp.float32) - analyzer_out.astype(jnp.float32))
    ).astype(jnp.bfloat16)
    gate_partial = jnp.sum(error.astype(jnp.float32)[:, None, :] * entry_out, axis=2)
    error_pad = jnp.concatenate([error, jnp.zeros((1, col_count), jnp.bfloat16)], axis=0)
    grad_slot = (row_gate[:, None] * error_pad[row_token].astype(jnp.float32)).astype(jnp.bfloat16)
    grad_slot = grad_slot.reshape(local_experts, expert_ranks, CAP, col_count)
    grad_in = lax.all_gather(to_experts(grad_slot), "tensor", axis=3, tiled=True)
    d_act = jnp.einsum("escd,efd->escf", grad_in, down_full, preferred_element_type=jnp.float32)
    sigmoid_pre = jax.nn.sigmoid(pre_gate)
    d_gate_pre = (d_act * pre_up * sigmoid_pre * (1.0 + pre_gate * (1.0 - sigmoid_pre))).astype(
        jnp.bfloat16
    )
    d_up_pre = (d_act * pre_gate * sigmoid_pre).astype(jnp.bfloat16)
    d_entry_part = jnp.einsum(
        "escf,edf->escd", d_gate_pre, gate_full, preferred_element_type=jnp.float32
    )
    d_entry_part = d_entry_part + jnp.einsum(
        "escf,edf->escd", d_up_pre, up_full, preferred_element_type=jnp.float32
    )
    d_entry_sum = lax.psum_scatter(
        d_entry_part.astype(jnp.bfloat16), "tensor", scatter_dimension=3, tiled=True
    )
    d_returned = to_tokens(d_entry_sum).reshape(slot_count, col_count)
    d_normed = jnp.sum(
        d_returned[dest_row].reshape(tok_count, top_count, col_count).astype(jnp.float32), axis=1
    )
    scaled = gain_cols * d_normed
    norm_partial = jnp.sum(scaled * hidden_cols, axis=1)
    norm_dots, gate_prob_grad = lax.psum((norm_partial, gate_partial), "tensor")
    cubed = inv_rms * inv_rms * inv_rms
    d_hidden = (
        error.astype(jnp.float32)
        + inv_rms * scaled
        - hidden_cols * cubed * norm_dots[:, None] / feature_count
    ).astype(jnp.bfloat16)
    context_grad = lax.dot_general(
        lax.all_gather(d_hidden, "tensor", axis=1, tiled=True),
        wo_rows,
        (((1,), (1,)), ((), ())),
        preferred_element_type=jnp.float32,
    ).astype(jnp.bfloat16)
    gate_up_part, down_part = weight_terms(arrived, activation, grad_in, d_gate_pre, d_up_pre)
    gate_up_kept, gate_up_arrived = dp_halves_sent(gate_up_part, dp_first, 2)
    down_kept, down_arrived = dp_halves_sent(down_part, dp_first, 2)
    gate_up_arrived, down_arrived, context_grad = lax.optimization_barrier(
        (gate_up_arrived, down_arrived, context_grad)
    )
    return (
        block_out,
        context_grad,
        gate_prob_grad,
        halves_added(gate_up_kept, gate_up_arrived),
        halves_added(down_kept, down_arrived),
    )


def solution(mesh):
    in_specs = (
        P(("dp", "expert"), "tensor"),
        P(("dp", "expert"), None),
        P("tensor", None),
        P(),
        P(("dp", "expert"), "tensor"),
        P(("dp", "expert"), None),
        P(("dp", "expert"), None),
        P("expert", None, "dp", "tensor"),
        P("expert", "tensor", "dp"),
    )
    out_specs = (
        P(("dp", "expert"), "tensor"),
        P(("dp", "expert"), "tensor"),
        P(("dp", "expert"), None),
        P("expert", None, "dp", "tensor"),
        P("expert", "tensor", "dp"),
    )
    return jax.shard_map(
        per_device, mesh=mesh, in_specs=in_specs, out_specs=out_specs, check_vma=False
    )
```

```python
import jax
import jax.numpy as jnp
from jax import lax
from jax.sharding import PartitionSpec as P

EXPERTS = 64
CAP = 14


NORM_EPS = 1e-06
LOSS_WEIGHT = 0.25


def to_experts(outgoing):
    return lax.all_to_all(outgoing, "expert", split_axis=1, concat_axis=1, tiled=True)


def to_tokens(outgoing):
    return lax.all_to_all(outgoing, "expert", split_axis=1, concat_axis=1, tiled=True)


DP_SWAP = [(0, 1), (1, 0)]


def tensor_shift(value, shift, count):
    return lax.ppermute(value, "tensor", [(j, (j + shift) % count) for j in range(count)])


def by_source(received, count):
    order = (lax.axis_index("tensor") - jnp.arange(count)) % count
    return jnp.take(jnp.stack(received), order, axis=0)


def tensor_pieces(value):
    count = lax.axis_size("tensor")
    received = [value] + [tensor_shift(value, shift, count) for shift in range(1, count)]
    return by_source(received, count)


def tensor_total(value):
    pieces = tensor_pieces(value)
    total = pieces[0]
    for member in range(1, pieces.shape[0]):
        total = total + pieces[member]
    return total


def tensor_scattered(value):
    count = lax.axis_size("tensor")
    width = value.shape[1] // count
    me = lax.axis_index("tensor")
    received = [lax.dynamic_slice_in_dim(value, me * width, width, 1)]
    for shift in range(1, count):
        sent = lax.dynamic_slice_in_dim(value, (me + shift) % count * width, width, 1)
        received.append(tensor_shift(sent, shift, count))
    pieces = by_source(received, count).astype(jnp.float32)
    total = pieces[0]
    for member in range(1, count):
        total = total + pieces[member]
    return total


def dp_joined(own, dp_first, axis):
    other = lax.ppermute(own, "dp", DP_SWAP)
    return jnp.where(
        dp_first,
        jnp.concatenate([own, other], axis=axis),
        jnp.concatenate([other, own], axis=axis),
    )


def dp_halves_sent(part, dp_first, axis):
    half = part.shape[axis] // 2
    low = lax.slice_in_dim(part, 0, half, axis=axis).astype(jnp.bfloat16)
    high = lax.slice_in_dim(part, half, 2 * half, axis=axis).astype(jnp.bfloat16)
    kept = jnp.where(dp_first, low, high)
    arrived = lax.ppermute(jnp.where(dp_first, high, low), "dp", DP_SWAP)
    return kept, arrived


def halves_added(kept, arrived):
    return (kept.astype(jnp.float32) + arrived.astype(jnp.float32)).astype(jnp.bfloat16)


def weight_terms(arrived, activation, grad_in, d_gate_pre, d_up_pre):
    down_part = jnp.einsum(
        "escf,escd->efd", activation, grad_in, preferred_element_type=jnp.float32
    )
    gate_part = jnp.einsum(
        "escd,escf->edf", arrived, d_gate_pre, preferred_element_type=jnp.float32
    )
    up_part = jnp.einsum("escd,escf->edf", arrived, d_up_pre, preferred_element_type=jnp.float32)
    return (jnp.stack([gate_part, up_part], axis=1), down_part)


def per_device(
    context, residual, wo_rows, norm_gain, analyzer_out, gate_probs, expert_ids, w_gate_up, w_down
):
    tok_count, top_count = expert_ids.shape
    feature_count = residual.shape[1]
    tensor_count = lax.axis_size("tensor")
    expert_ranks = lax.axis_size("expert")
    col_count = feature_count // tensor_count
    col_start = lax.axis_index("tensor") * col_count
    local_experts = w_gate_up.shape[0]
    slot_count = EXPERTS * CAP
    expert_range = jnp.arange(EXPERTS, dtype=jnp.int32)
    slot_order = expert_range % local_experts * expert_ranks + expert_range // local_experts
    dp_first = lax.axis_index("dp") == 0
    down_other = lax.ppermute(w_down, "dp", DP_SWAP)
    partial_attn = jnp.dot(context, wo_rows, preferred_element_type=jnp.float32)
    attn_cols = tensor_scattered(partial_attn.astype(jnp.bfloat16))
    hidden_cols = lax.dynamic_slice_in_dim(residual, col_start, col_count, 1).astype(
        jnp.float32
    ) + attn_cols
    square_sum = tensor_total(jnp.sum(hidden_cols * hidden_cols, axis=1, keepdims=True))
    inv_rms = lax.rsqrt(square_sum / feature_count + NORM_EPS)
    gain_cols = lax.dynamic_slice_in_dim(norm_gain, col_start, col_count, 0)
    normed = (gain_cols * hidden_cols * inv_rms).astype(jnp.bfloat16)
    flat_ids = expert_ids.reshape(-1)
    onehot = (flat_ids[:, None] == expert_range[None, :]).astype(jnp.int32)
    slot_index = jnp.sum((jnp.cumsum(onehot, axis=0) - onehot) * onehot, axis=1)
    expert_slot = jnp.sum(onehot * slot_order[None, :], axis=1)
    dest_row = expert_slot * CAP + slot_index
    sentinel = tok_count * top_count
    row_entry = (
        jnp.full((slot_count,), sentinel, jnp.int32)
        .at[dest_row]
        .set(jnp.arange(sentinel, dtype=jnp.int32))
    )
    row_token = row_entry // top_count
    gate_pad = jnp.concatenate([gate_probs.reshape(-1), jnp.zeros((1,), jnp.float32)])
    row_gate = gate_pad[row_entry]
    normed_pad = jnp.concatenate([normed, jnp.zeros((1, col_count), jnp.bfloat16)], axis=0)
    outgoing = normed_pad[row_token].reshape(local_experts, expert_ranks, CAP, col_count)
    first_other = lax.ppermute(w_gate_up[0:1, 0:1], "dp", DP_SWAP)
    down_other, first_other, outgoing = lax.optimization_barrier(
        (down_other, first_other, outgoing)
    )
    second_other = lax.ppermute(w_gate_up[0:1, 1:2], "dp", DP_SWAP)
    rest_other = lax.ppermute(w_gate_up[1:], "dp", DP_SWAP)
    gate_up_other = jnp.concatenate(
        [jnp.concatenate([first_other, second_other], axis=1), rest_other], axis=0
    )
    gate_up_full = jnp.where(
        dp_first,
        jnp.concatenate([w_gate_up, gate_up_other], axis=2),
        jnp.concatenate([gate_up_other, w_gate_up], axis=2),
    )
    down_full = jnp.where(
        dp_first,
        jnp.concatenate([w_down, down_other], axis=2),
        jnp.concatenate([down_other, w_down], axis=2),
    )
    arrived = lax.all_gather(to_experts(outgoing), "tensor", axis=3, tiled=True)
    gate_full = gate_up_full[:, 0]
    up_full = gate_up_full[:, 1]
    half_count = feature_count // 2
    dp_index = lax.axis_index("dp")
    own_rows = lax.dynamic_slice_in_dim(arrived, dp_index * half_count, half_count, 3)
    other_rows = lax.dynamic_slice_in_dim(arrived, (1 - dp_index) * half_count, half_count, 3)
    other_pieces = ((first_other[0, 0], second_other[0, 0]), (rest_other[0, 0], rest_other[0, 1]))

    def projected(which):
        return jnp.stack(
            [
                jnp.einsum(
                    "scd,df->scf", own_rows[e], w_gate_up[e, which],
                    preferred_element_type=jnp.float32,
                )
                + jnp.einsum(
                    "scd,df->scf", other_rows[e], other_pieces[e][which],
                    preferred_element_type=jnp.float32,
                )
                for e in range(local_experts)
            ]
        )

    pre_gate = projected(0)
    pre_up = projected(1)
    activation = (jax.nn.silu(pre_gate) * pre_up).astype(jnp.bfloat16)
    partial_out = jnp.einsum(
        "escf,efd->escd", activation, down_full, preferred_element_type=jnp.float32
    )
    summed_out = lax.psum_scatter(
        partial_out.astype(jnp.bfloat16), "tensor", scatter_dimension=3, tiled=True
    )
    returned = to_tokens(summed_out).reshape(slot_count, col_count)
    entry_out = returned[dest_row].reshape(tok_count, top_count, col_count).astype(jnp.float32)
    block_out = (hidden_cols + jnp.sum(gate_probs[:, :, None] * entry_out, axis=1)).astype(
        jnp.bfloat16
    )
    error = (
        LOSS_WEIGHT * (block_out.astype(jnp.float32) - analyzer_out.astype(jnp.float32))
    ).astype(jnp.bfloat16)
    gate_partial = jnp.sum(error.astype(jnp.float32)[:, None, :] * entry_out, axis=2)
    error_pad = jnp.concatenate([error, jnp.zeros((1, col_count), jnp.bfloat16)], axis=0)
    grad_slot = (row_gate[:, None] * error_pad[row_token].astype(jnp.float32)).astype(jnp.bfloat16)
    grad_slot = grad_slot.reshape(local_experts, expert_ranks, CAP, col_count)
    grad_in = lax.all_gather(to_experts(grad_slot), "tensor", axis=3, tiled=True)
    d_act = jnp.einsum("escd,efd->escf", grad_in, down_full, preferred_element_type=jnp.float32)
    sigmoid_pre = jax.nn.sigmoid(pre_gate)
    d_gate_pre = (d_act * pre_up * sigmoid_pre * (1.0 + pre_gate * (1.0 - sigmoid_pre))).astype(
        jnp.bfloat16
    )
    d_up_pre = (d_act * pre_gate * sigmoid_pre).astype(jnp.bfloat16)
    d_entry_part = jnp.einsum(
        "escf,edf->escd", d_gate_pre, gate_full, preferred_element_type=jnp.float32
    )
    d_entry_part = d_entry_part + jnp.einsum(
        "escf,edf->escd", d_up_pre, up_full, preferred_element_type=jnp.float32
    )
    d_entry_sum = lax.psum_scatter(
        d_entry_part.astype(jnp.bfloat16), "tensor", scatter_dimension=3, tiled=True
    )
    d_returned = to_tokens(d_entry_sum).reshape(slot_count, col_count)
    d_normed = jnp.sum(
        d_returned[dest_row].reshape(tok_count, top_count, col_count).astype(jnp.float32), axis=1
    )
    scaled = gain_cols * d_normed
    norm_partial = jnp.sum(scaled * hidden_cols, axis=1)
    norm_dots, gate_prob_grad = lax.psum((norm_partial, gate_partial), "tensor")
    cubed = inv_rms * inv_rms * inv_rms
    d_hidden = (
        error.astype(jnp.float32)
        + inv_rms * scaled
        - hidden_cols * cubed * norm_dots[:, None] / feature_count
    ).astype(jnp.bfloat16)
    context_grad = lax.dot_general(
        lax.all_gather(d_hidden, "tensor", axis=1, tiled=True),
        wo_rows,
        (((1,), (1,)), ((), ())),
        preferred_element_type=jnp.float32,
    ).astype(jnp.bfloat16)
    gate_up_part, down_part = weight_terms(arrived, activation, grad_in, d_gate_pre, d_up_pre)
    gate_up_kept, gate_up_arrived = dp_halves_sent(gate_up_part, dp_first, 2)
    down_kept, down_arrived = dp_halves_sent(down_part, dp_first, 2)
    gate_up_arrived, down_arrived, context_grad = lax.optimization_barrier(
        (gate_up_arrived, down_arrived, context_grad)
    )
    return (
        block_out,
        context_grad,
        gate_prob_grad,
        halves_added(gate_up_kept, gate_up_arrived),
        halves_added(down_kept, down_arrived),
    )


def solution(mesh):
    in_specs = (
        P(("dp", "expert"), "tensor"),
        P(("dp", "expert"), None),
        P("tensor", None),
        P(),
        P(("dp", "expert"), "tensor"),
        P(("dp", "expert"), None),
        P(("dp", "expert"), None),
        P("expert", None, "dp", "tensor"),
        P("expert", "tensor", "dp"),
    )
    out_specs = (
        P(("dp", "expert"), "tensor"),
        P(("dp", "expert"), "tensor"),
        P(("dp", "expert"), None),
        P("expert", None, "dp", "tensor"),
        P("expert", "tensor", "dp"),
    )
    return jax.shard_map(
        per_device, mesh=mesh, in_specs=in_specs, out_specs=out_specs, check_vma=False
    )
```
